512 devices in a mesh: ops: 16 (over x, y), sec: 32 (over z, core).
Axes of the slice: x: 4, y: 4, z: 16, core: 2. Of those that a mesh axis runs over, the one named last changes fastest.
Arguments:
- wave: bfloat16 [32, 768, 768], P('sec')
- left_ops: bfloat16 [16, 32, 768, 768], P('ops', 'sec'), may hold values from -0.21875 to 0.21875
- right_ops: bfloat16 [16, 32, 768, 768], P('ops', 'sec'), may hold values from -0.21875 to 0.21875
- priors: bfloat16 [8, 32, 768, 768], P(None, 'sec', 'ops'), as said below
- row_sizes: int32 [32], P('sec'), may hold values from 64 to 768, as said below
- col_sizes: int32 [32], P('sec'), may hold values from 64 to 768, as said below
Outputs:
- sigma: bfloat16 [32, 768, 768], P('sec', 'ops')
- new_dir: bfloat16 [32, 768, 768], P('sec', 'ops')
- correlations: float32 [8], replicated
The draws below stay inside these ranges and needn't reach their ends.
Inputs may be any that keep to these rules, and one draw needn't show every extreme that they name: `row_sizes`: one sector's block uses all 768 rows. `col_sizes`: one sector's block uses all 768 columns. `priors`: each prior vector has a norm of about one over all cells.
All inputs are finite; a program needn't handle non-finite values.
Results may differ from the reference program's by a relative error of at most 0.012.
Values sent between devices are 32-bit elements; how exact they have to be, the bound alone decides.
No kernel may reach another device: no remote copies, remote signals or barrier semaphores. Data moves between devices by JAX's collectives and lax.ppermute only.
A program may use at most 64 MiB of HBM per device.

```python
import jax
import jax.numpy as jnp
from jax import lax

B = 768
NPRIOR = 8
TERMS = 16
SECTORS = 32


def draw_wave(key, part):
    key_a, key_b = jax.random.split(jax.random.fold_in(key, 11), 2)
    rough = jax.random.normal(key_a, (SECTORS, B, B), jnp.float32)
    scales = jnp.exp(jax.random.uniform(key_b, (SECTORS, B, 1), jnp.float32, 0.0, 2.3))
    rising = 3.0 ** (jnp.arange(SECTORS, dtype=jnp.float32) / max(SECTORS - 1, 1))
    values = rough * scales * rising[:, None, None] * 0.3
    return jnp.clip(values, -12.0, 12.0).astype(jnp.bfloat16)


def draw_priors(key, part):
    key_a = jax.random.fold_in(jax.random.fold_in(key, 53), 0)
    norm_scale = (SECTORS * B * B) ** (-0.5)
    rough = jax.random.normal(key_a, (NPRIOR, SECTORS, B, B), jnp.float32)
    values = jnp.clip(rough, -6.0, 6.0) * norm_scale
    return values.astype(jnp.bfloat16)


def block_sizes(key, salt):
    key_a, key_b, key_c = jax.random.split(jax.random.fold_in(key, salt), 3)
    lowest = min(64, B // 4)
    span = B - lowest + 1
    first = jax.random.randint(key_a, (SECTORS,), 0, span)
    second = jax.random.randint(key_b, (SECTORS,), 0, span)
    sizes = lowest + first * second // span
    widest = jax.random.randint(key_c, (), 0, SECTORS)
    return jnp.where(jnp.arange(SECTORS) == widest, B, sizes).astype(jnp.int32)


def draw_row_sizes(key, part):
    return block_sizes(key, 23)


def draw_col_sizes(key, part):
    return block_sizes(key, 37)


def steps_of(rng, dims, pieces, low, largest):
    loudness, own = 1.0, jax.random.fold_in(rng, 6)
    for axis_at, blocks in pieces:
        heights = jnp.exp(jax.random.uniform(jax.random.fold_in(own, axis_at), (blocks,), jnp.float32, low / len(pieces), largest / len(pieces)))
        loudness = loudness * jnp.repeat(heights, dims[axis_at] // blocks).reshape([-1 if axis == axis_at else 1 for axis in range(len(dims))])
    return loudness


def noise(rng, extent, scale, bound, shards=(), kind=jnp.bfloat16):
    entries = scale * jax.random.normal(rng, extent, jnp.float32)
    if shards:
        entries = entries * steps_of(rng, extent, shards, -0.22, 0.18)
    return jnp.clip(entries, -bound, bound).astype(kind)


def setup_inputs(seed: int = 0) -> dict:
    key_list = jax.random.split(jax.random.key(seed), 7)
    return {
        "wave": draw_wave(jax.random.fold_in(key_list[6], 71), 0),
        "left_ops": noise(key_list[1], (TERMS, SECTORS, B, B), B ** -0.5, 0.21875, ((0, 16), (1, 32))),
        "right_ops": noise(key_list[2], (TERMS, SECTORS, B, B), B ** -0.5, 0.21875, ((0, 16), (1, 32))),
        "priors": draw_priors(jax.random.fold_in(key_list[6], 71), 0),
        "row_sizes": draw_row_sizes(jax.random.fold_in(key_list[6], 71), 0),
        "col_sizes": draw_col_sizes(jax.random.fold_in(key_list[6], 71), 0),
    }


def reference(wave, left_ops, right_ops, priors, row_sizes, col_sizes):
    count = wave.shape[0]
    width = wave.shape[1]
    place = jnp.arange(width, dtype=jnp.int32)
    row_mask = (place[None, :] < row_sizes[:, None]).astype(jnp.float32)
    col_mask = (place[None, :] < col_sizes[:, None]).astype(jnp.float32)
    mask = row_mask[:, :, None] * col_mask[:, None, :]
    masked = wave * mask.astype(jnp.bfloat16)

    def sector(items):
        block, lefts, rights, cells = items

        def add_term(total, pair):
            left, right = pair
            inner = jnp.dot(block, right.T, preferred_element_type=jnp.float32).astype(jnp.bfloat16)
            return (total + jnp.dot(left, inner, preferred_element_type=jnp.float32), None)
        total, unused = lax.scan(add_term, jnp.zeros((width, width), jnp.float32), (lefts, rights))
        return (total * cells).astype(jnp.bfloat16)
    sigma = lax.map(sector, (masked, jnp.swapaxes(left_ops, 0, 1), jnp.swapaxes(right_ops, 0, 1), mask))
    pmask = (priors * mask[None].astype(jnp.bfloat16)).astype(jnp.float32)
    sig32 = sigma.astype(jnp.float32)
    correlations = jnp.einsum('psab,sab->p', pmask, sig32, precision=lax.Precision.HIGHEST)
    resid = sig32 - jnp.einsum('p,psab->sab', correlations, pmask, precision=lax.Precision.HIGHEST)
    msq = jnp.sum(resid * resid) / (count * width * width)
    new_dir = (resid / jnp.sqrt(msq + 1e-06)).astype(jnp.bfloat16)
    return (sigma, new_dir, correlations)
```

```python
import jax
import jax.numpy as jnp
from jax import lax
from jax.sharding import PartitionSpec as P


def reduce_rows(partial, shard_rows):
    n = lax.axis_size("ops")
    blocks = partial.reshape(n, shard_rows, partial.shape[2])
    got = lax.all_to_all(blocks, "ops", 0, 0, tiled=True)
    return jnp.sum(got, axis=0, keepdims=True)


def small_sum(v):
    for ax in ("ops", "sec"):
        n = lax.axis_size(ax)
        x = jnp.broadcast_to(v.reshape(1, -1), (n, v.size))
        v = jnp.sum(lax.all_to_all(x, ax, 0, 0, tiled=True), axis=0).reshape(v.shape)
    return v


def shards(wave, left_ops, right_ops, priors, row_sizes, col_sizes):
    width = wave.shape[1]
    sec_local = wave.shape[0]
    shard_rows = width // lax.axis_size("ops")
    first_row = lax.axis_index("ops") * shard_rows
    place = jnp.arange(width, dtype=jnp.int32)
    row_mask = (place[None, :] < row_sizes[:, None]).astype(jnp.float32)
    col_mask = (place[None, :] < col_sizes[:, None]).astype(jnp.float32)
    full_mask = row_mask[:, :, None] * col_mask[:, None, :]
    masked = wave * full_mask.astype(jnp.bfloat16)
    inner = jnp.einsum(
        "sab,ksjb->ksaj", masked, right_ops, preferred_element_type=jnp.float32
    ).astype(jnp.bfloat16)
    partial_all = jnp.einsum("ksia,ksaj->sij", left_ops, inner, preferred_element_type=jnp.float32)
    summed = reduce_rows(partial_all, shard_rows)
    mine_rows = lax.dynamic_slice_in_dim(row_mask, first_row, shard_rows, 1)
    mine_mask = mine_rows[:, :, None] * col_mask[:, None, :]
    sigma = (summed * mine_mask).astype(jnp.bfloat16)
    pmask = (priors * mine_mask[None].astype(jnp.bfloat16)).astype(jnp.float32)
    sig32 = sigma.astype(jnp.float32)
    local_over = jnp.einsum("psab,sab->p", pmask, sig32, precision=lax.Precision.HIGHEST)
    correlations = small_sum(local_over)
    resid = sig32 - jnp.einsum("p,psab->sab", correlations, pmask, precision=lax.Precision.HIGHEST)
    total = small_sum(jnp.sum(resid * resid))
    cells = sec_local * lax.axis_size("sec") * width * width
    new_dir = (resid / jnp.sqrt(total / cells + 1e-06)).astype(jnp.bfloat16)
    return (sigma, new_dir, correlations)


def solution(mesh):
    in_specs = (
        P("sec", None, None),
        P("ops", "sec", None, None),
        P("ops", "sec", None, None),
        P(None, "sec", "ops", None),
        P("sec"),
        P("sec"),
    )
    out_specs = (P("sec", "ops", None), P("sec", "ops", None), P())
    return jax.shard_map(shards, mesh=mesh, in_specs=in_specs, out_specs=out_specs, check_vma=False)
```

```python
import jax
import jax.numpy as jnp
from jax import lax
from jax.sharding import PartitionSpec as P


def reduce_rows(partial, shard_rows):
    n = lax.axis_size("ops")
    blocks = partial.reshape(n, shard_rows, partial.shape[2])
    got = lax.all_to_all(blocks, "ops", 0, 0, tiled=True)
    return jnp.sum(got, axis=0, keepdims=True)


def small_sum(v):
    for ax in ("ops", "sec"):
        n = lax.axis_size(ax)
        x = jnp.broadcast_to(v.reshape(1, -1), (n, v.size))
        v = jnp.sum(lax.all_to_all(x, ax, 0, 0, tiled=True), axis=0).reshape(v.shape)
    return v


def shards(wave, left_ops, right_ops, priors, row_sizes, col_sizes):
    width = wave.shape[1]
    sec_local = wave.shape[0]
    shard_rows = width // lax.axis_size("ops")
    first_row = lax.axis_index("ops") * shard_rows
    place = jnp.arange(width, dtype=jnp.int32)
    row_mask = (place[None, :] < row_sizes[:, None]).astype(jnp.float32)
    col_mask = (place[None, :] < col_sizes[:, None]).astype(jnp.float32)
    full_mask = row_mask[:, :, None] * col_mask[:, None, :]
    masked = wave * full_mask.astype(jnp.bfloat16)
    inner = jnp.einsum(
        "sab,ksjb->ksaj", masked, right_ops, preferred_element_type=jnp.float32
    ).astype(jnp.bfloat16)
    partial_all = jnp.einsum("ksia,ksaj->sij", left_ops, inner, preferred_element_type=jnp.float32)
    summed = reduce_rows(partial_all, shard_rows)
    mine_rows = lax.dynamic_slice_in_dim(row_mask, first_row, shard_rows, 1)
    mine_mask = mine_rows[:, :, None] * col_mask[:, None, :]
    sigma = (summed * mine_mask).astype(jnp.bfloat16)
    pmask = (priors * mine_mask[None].astype(jnp.bfloat16)).astype(jnp.float32)
    sig32 = sigma.astype(jnp.float32)
    local_over = jnp.einsum("psab,sab->p", pmask, sig32, precision=lax.Precision.HIGHEST)
    gram = jnp.einsum("psab,qsab->pq", pmask, pmask, precision=lax.Precision.HIGHEST)
    sig_sq = jnp.sum(sig32 * sig32)
    nprior = local_over.shape[0]
    packed = jnp.concatenate([local_over, gram.reshape(-1), sig_sq[None]])
    sums = small_sum(packed)
    correlations = sums[:nprior]
    gram_all = sums[nprior:-1].reshape(nprior, nprior)
    sig_sq_all = sums[-1]
    resid = sig32 - jnp.einsum("p,psab->sab", correlations, pmask, precision=lax.Precision.HIGHEST)
    expanded = (
        sig_sq_all
        - 2.0 * jnp.dot(correlations, correlations, precision=lax.Precision.HIGHEST)
        + jnp.dot(
            correlations,
            jnp.dot(gram_all, correlations, precision=lax.Precision.HIGHEST),
            precision=lax.Precision.HIGHEST,
        )
    )
    total = lax.cond(
        expanded >= sig_sq_all * 0.0625,
        lambda r: expanded,
        lambda r: small_sum(jnp.sum(r * r)),
        resid,
    )
    cells = sec_local * lax.axis_size("sec") * width * width
    new_dir = (resid / jnp.sqrt(total / cells + 1e-06)).astype(jnp.bfloat16)
    return (sigma, new_dir, correlations)


def solution(mesh):
    in_specs = (
        P("sec", None, None),
        P("ops", "sec", None, None),
        P("ops", "sec", None, None),
        P(None, "sec", "ops", None),
        P("sec"),
        P("sec"),
    )
    out_specs = (P("sec", "ops", None), P("sec", "ops", None), P())
    return jax.shard_map(shards, mesh=mesh, in_specs=in_specs, out_specs=out_specs, check_vma=False)
```

```python
import jax
import jax.numpy as jnp
from jax import lax
from jax.sharding import PartitionSpec as P


def reduce_rows(partial, shard_rows):
    n = lax.axis_size("ops")
    blocks = partial.reshape(n, shard_rows, partial.shape[2])
    got = lax.all_to_all(blocks, "ops", 0, 0, tiled=True)
    return jnp.sum(got, axis=0, keepdims=True)


def small_sum(v):
    for ax in ("sec", "ops"):
        n = lax.axis_size(ax)
        x = jnp.broadcast_to(v.reshape(1, -1), (n, v.size))
        v = jnp.sum(lax.all_to_all(x, ax, 0, 0, tiled=True), axis=0).reshape(v.shape)
    return v


def shards(wave, left_ops, right_ops, priors, row_sizes, col_sizes):
    width = wave.shape[1]
    sec_local = wave.shape[0]
    shard_rows = width // lax.axis_size("ops")
    first_row = lax.axis_index("ops") * shard_rows
    place = jnp.arange(width, dtype=jnp.int32)
    row_mask = (place[None, :] < row_sizes[:, None]).astype(jnp.float32)
    col_mask = (place[None, :] < col_sizes[:, None]).astype(jnp.float32)
    full_mask = row_mask[:, :, None] * col_mask[:, None, :]
    masked = wave * full_mask.astype(jnp.bfloat16)
    inner = jnp.einsum(
        "sab,ksjb->ksaj", masked, right_ops, preferred_element_type=jnp.float32
    ).astype(jnp.bfloat16)
    partial_all = jnp.einsum("ksia,ksaj->sij", left_ops, inner, preferred_element_type=jnp.float32)
    summed = reduce_rows(partial_all, shard_rows)
    mine_rows = lax.dynamic_slice_in_dim(row_mask, first_row, shard_rows, 1)
    mine_mask = mine_rows[:, :, None] * col_mask[:, None, :]
    own_rows = first_row + jnp.arange(shard_rows, dtype=jnp.int32)
    prior_ok = (own_rows[None, :, None] + 1 <= row_sizes[:, None, None]) & (
        place[None, None, :] + 1 <= col_sizes[:, None, None]
    )
    pmask = jnp.where(prior_ok[None], priors, jnp.zeros_like(priors)).astype(jnp.float32)
    gram = jnp.einsum("psab,qsab->pq", pmask, pmask, precision=lax.Precision.HIGHEST)
    sigma = (summed * mine_mask).astype(jnp.bfloat16)
    sig32 = sigma.astype(jnp.float32)
    local_over = jnp.einsum("psab,sab->p", pmask, sig32, precision=lax.Precision.HIGHEST)
    sig_sq = jnp.sum(sig32 * sig32)
    nprior = local_over.shape[0]
    packed = jnp.concatenate([local_over, gram.reshape(-1), sig_sq[None]])
    sums = small_sum(packed)
    correlations = sums[:nprior]
    gram_all = sums[nprior:-1].reshape(nprior, nprior)
    sig_sq_all = sums[-1]
    resid = sig32 - jnp.einsum("p,psab->sab", correlations, pmask, precision=lax.Precision.HIGHEST)
    expanded = (
        sig_sq_all
        - 2.0 * jnp.dot(correlations, correlations, precision=lax.Precision.HIGHEST)
        + jnp.dot(
            correlations,
            jnp.dot(gram_all, correlations, precision=lax.Precision.HIGHEST),
            precision=lax.Precision.HIGHEST,
        )
    )
    total = lax.cond(
        expanded >= sig_sq_all * 0.0625,
        lambda r: expanded,
        lambda r: small_sum(jnp.sum(r * r)),
        resid,
    )
    cells = sec_local * lax.axis_size("sec") * width * width
    new_dir = (resid / jnp.sqrt(total / cells + 1e-06)).astype(jnp.bfloat16)
    return (sigma, new_dir, correlations)


def solution(mesh):
    in_specs = (
        P("sec", None, None),
        P("ops", "sec", None, None),
        P("ops", "sec", None, None),
        P(None, "sec", "ops", None),
        P("sec"),
        P("sec"),
    )
    out_specs = (P("sec", "ops", None), P("sec", "ops", None), P())
    return jax.shard_map(shards, mesh=mesh, in_specs=in_specs, out_specs=out_specs, check_vma=False)
```

```python
import jax
import jax.numpy as jnp
from jax import lax
from jax.sharding import PartitionSpec as P


def reduce_rows(partial, shard_rows):
    n = lax.axis_size("ops")
    blocks = partial.reshape(n, shard_rows, partial.shape[2])
    got = lax.all_to_all(blocks, "ops", 0, 0, tiled=True)
    return jnp.sum(got, axis=0, keepdims=True)


def small_sum(v):
    for ax in ("sec", "ops"):
        n = lax.axis_size(ax)
        x = jnp.broadcast_to(v.reshape(1, -1), (n, v.size))
        v = jnp.sum(lax.all_to_all(x, ax, 0, 0, tiled=True), axis=0).reshape(v.shape)
    return v


def shards(wave, left_ops, right_ops, priors, row_sizes, col_sizes):
    width = wave.shape[1]
    sec_local = wave.shape[0]
    shard_rows = width // lax.axis_size("ops")
    first_row = lax.axis_index("ops") * shard_rows
    place = jnp.arange(width, dtype=jnp.int32)
    row_mask = (place[None, :] < row_sizes[:, None]).astype(jnp.float32)
    col_mask = (place[None, :] < col_sizes[:, None]).astype(jnp.float32)
    full_mask = row_mask[:, :, None] * col_mask[:, None, :]
    masked = wave * full_mask.astype(jnp.bfloat16)
    inner = jnp.einsum(
        "sab,ksjb->ksaj", masked, right_ops, preferred_element_type=jnp.float32
    ).astype(jnp.bfloat16)
    partial_all = jnp.einsum("ksia,ksaj->sij", left_ops, inner, preferred_element_type=jnp.float32)
    summed = reduce_rows(partial_all, shard_rows)
    mine_rows = lax.dynamic_slice_in_dim(row_mask, first_row, shard_rows, 1)
    mine_mask = mine_rows[:, :, None] * col_mask[:, None, :]
    own_rows = first_row + jnp.arange(shard_rows, dtype=jnp.int32)
    prior_ok = (own_rows[None, :, None] + 1 <= row_sizes[:, None, None]) & (
        place[None, None, :] + 1 <= col_sizes[:, None, None]
    )
    pmask = jnp.where(prior_ok[None], priors, jnp.zeros_like(priors)).astype(jnp.float32)
    gram = jnp.einsum("psab,qsab->pq", pmask, pmask, precision=lax.Precision.HIGHEST)
    sigma = (summed * mine_mask).astype(jnp.bfloat16)
    sig32 = sigma.astype(jnp.float32)
    local_over = jnp.sum(pmask * sig32[None], axis=(1, 2, 3))
    sig_sq = jnp.sum(sig32 * sig32)
    nprior = local_over.shape[0]
    packed = jnp.concatenate([local_over, gram.reshape(-1), sig_sq[None]])
    sums = small_sum(packed)
    correlations = sums[:nprior]
    gram_all = sums[nprior:-1].reshape(nprior, nprior)
    sig_sq_all = sums[-1]
    resid = sig32 - jnp.sum(correlations[:, None, None, None] * pmask, axis=0)
    expanded = (
        sig_sq_all
        - 2.0 * jnp.dot(correlations, correlations, precision=lax.Precision.HIGHEST)
        + jnp.dot(
            correlations,
            jnp.dot(gram_all, correlations, precision=lax.Precision.HIGHEST),
            precision=lax.Precision.HIGHEST,
        )
    )
    total = lax.cond(
        expanded >= sig_sq_all * 0.0625,
        lambda r: expanded,
        lambda r: small_sum(jnp.sum(r * r)),
        resid,
    )
    cells = sec_local * lax.axis_size("sec") * width * width
    new_dir = (resid / jnp.sqrt(total / cells + 1e-06)).astype(jnp.bfloat16)
    return (sigma, new_dir, correlations)


def solution(mesh):
    in_specs = (
        P("sec", None, None),
        P("ops", "sec", None, None),
        P("ops", "sec", None, None),
        P(None, "sec", "ops", None),
        P("sec"),
        P("sec"),
    )
    out_specs = (P("sec", "ops", None), P("sec", "ops", None), P())
    return jax.shard_map(shards, mesh=mesh, in_specs=in_specs, out_specs=out_specs, check_vma=False)
```

```python
import jax
import jax.numpy as jnp
from jax import lax
from jax.sharding import PartitionSpec as P


def reduce_rows(partial, shard_rows):
    n = lax.axis_size("ops")
    blocks = partial.reshape(n, shard_rows, partial.shape[2])
    got = lax.all_to_all(blocks, "ops", 0, 0, tiled=True)
    return jnp.sum(got, axis=0, keepdims=True)


def small_sum(v):
    for ax in ("sec", "ops"):
        n = lax.axis_size(ax)
        x = jnp.broadcast_to(v.reshape(1, -1), (n, v.size))
        v = jnp.sum(lax.all_to_all(x, ax, 0, 0, tiled=True), axis=0).reshape(v.shape)
    return v


def shards(wave, left_ops, right_ops, priors, row_sizes, col_sizes):
    width = wave.shape[1]
    sec_local = wave.shape[0]
    shard_rows = width // lax.axis_size("ops")
    first_row = lax.axis_index("ops") * shard_rows
    place = jnp.arange(width, dtype=jnp.int32)
    row_mask = (place[None, :] < row_sizes[:, None]).astype(jnp.float32)
    col_mask = (place[None, :] < col_sizes[:, None]).astype(jnp.float32)
    full_mask = row_mask[:, :, None] * col_mask[:, None, :]
    masked = wave * full_mask.astype(jnp.bfloat16)
    inner = jnp.einsum(
        "sab,ksjb->ksaj", masked, right_ops, preferred_element_type=jnp.float32
    ).astype(jnp.bfloat16)
    partial_all = jnp.einsum("ksia,ksaj->sij", left_ops, inner, preferred_element_type=jnp.float32)
    summed = reduce_rows(partial_all, shard_rows)
    mine_rows = lax.dynamic_slice_in_dim(row_mask, first_row, shard_rows, 1)
    mine_mask = mine_rows[:, :, None] * col_mask[:, None, :]
    own_rows = first_row + jnp.arange(shard_rows, dtype=jnp.int32)
    prior_ok = (own_rows[None, :, None] + 1 <= row_sizes[:, None, None]) & (
        place[None, None, :] + 1 <= col_sizes[:, None, None]
    )
    pmask = jnp.where(prior_ok[None], priors, jnp.zeros_like(priors)).astype(jnp.float32)
    gram = jnp.einsum("psab,qsab->pq", pmask, pmask, precision=lax.Precision.HIGHEST)
    sigma = (summed * mine_mask).astype(jnp.bfloat16)
    sig32 = sigma.astype(jnp.float32)
    local_over = jnp.sum(pmask * sig32[None], axis=(1, 2, 3))
    sig_sq = jnp.sum(sig32 * sig32)
    nprior = local_over.shape[0]
    packed = jnp.concatenate([local_over, gram.reshape(-1), sig_sq[None]])
    sums = small_sum(packed)
    correlations = sums[:nprior]
    gram_all = sums[nprior:-1].reshape(nprior, nprior)
    sig_sq_all = sums[-1]
    resid = sig32 - jnp.sum(correlations[:, None, None, None] * pmask, axis=0)
    eye = jnp.eye(nprior, dtype=jnp.float32)
    expanded = sig_sq_all + jnp.sum(correlations[:, None] * correlations[None, :] * (gram_all - 2.0 * eye))
    cells = sec_local * lax.axis_size("sec") * width * width

    def scaled(total):
        return (resid / jnp.sqrt(total / cells + 1e-06)).astype(jnp.bfloat16)

    fast = scaled(expanded)
    new_dir = lax.cond(
        expanded >= sig_sq_all * 0.0625,
        lambda r: fast,
        lambda r: scaled(small_sum(jnp.sum(r * r))),
        resid,
    )
    return (sigma, new_dir, correlations)


def solution(mesh):
    in_specs = (
        P("sec", None, None),
        P("ops", "sec", None, None),
        P("ops", "sec", None, None),
        P(None, "sec", "ops", None),
        P("sec"),
        P("sec"),
    )
    out_specs = (P("sec", "ops", None), P("sec", "ops", None), P())
    return jax.shard_map(shards, mesh=mesh, in_specs=in_specs, out_specs=out_specs, check_vma=False)
```

```python
import jax
import jax.numpy as jnp
from jax import lax
from jax.sharding import PartitionSpec as P


def reduce_rows(partial, shard_rows):
    n = lax.axis_size("ops")
    blocks = partial.reshape(n, shard_rows, partial.shape[2])
    got = lax.all_to_all(blocks, "ops", 0, 0, tiled=True)
    return jnp.sum(got, axis=0, keepdims=True)


def small_sum(v):
    for ax in ("sec", "ops"):
        n = lax.axis_size(ax)
        x = jnp.broadcast_to(v.reshape(1, -1), (n, v.size))
        v = jnp.sum(lax.all_to_all(x, ax, 0, 0, tiled=True), axis=0).reshape(v.shape)
    return v


def shards(wave, left_ops, right_ops, priors, row_sizes, col_sizes):
    width = wave.shape[1]
    sec_local = wave.shape[0]
    shard_rows = width // lax.axis_size("ops")
    first_row = lax.axis_index("ops") * shard_rows
    place = jnp.arange(width, dtype=jnp.int32)
    row_mask = (place[None, :] < row_sizes[:, None]).astype(jnp.float32)
    col_mask = (place[None, :] < col_sizes[:, None]).astype(jnp.float32)
    full_mask = row_mask[:, :, None] * col_mask[:, None, :]
    masked = wave * full_mask.astype(jnp.bfloat16)
    inner = lax.dot_general(
        masked[0], right_ops[0, 0], (((1,), (1,)), ((), ())), preferred_element_type=jnp.float32
    ).astype(jnp.bfloat16)
    partial_all = jnp.dot(left_ops[0, 0], inner, preferred_element_type=jnp.float32)[None]
    summed = reduce_rows(partial_all, shard_rows)
    mine_rows = lax.dynamic_slice_in_dim(row_mask, first_row, shard_rows, 1)
    mine_mask = mine_rows[:, :, None] * col_mask[:, None, :]
    own_rows = first_row + jnp.arange(shard_rows, dtype=jnp.int32)
    prior_ok = (own_rows[None, :, None] + 1 <= row_sizes[:, None, None]) & (
        place[None, None, :] + 1 <= col_sizes[:, None, None]
    )
    pmask = jnp.where(prior_ok[None], priors, jnp.zeros_like(priors)).astype(jnp.float32)
    gram = jnp.einsum("psab,qsab->pq", pmask, pmask, precision=lax.Precision.HIGHEST)
    sigma = (summed * mine_mask).astype(jnp.bfloat16)
    sig32 = sigma.astype(jnp.float32)
    local_over = jnp.sum(pmask * sig32[None], axis=(1, 2, 3))
    sig_sq = jnp.sum(sig32 * sig32)
    nprior = local_over.shape[0]
    packed = jnp.concatenate([local_over, gram.reshape(-1), sig_sq[None]])
    sums = small_sum(packed)
    correlations = sums[:nprior]
    gram_all = sums[nprior:-1].reshape(nprior, nprior)
    sig_sq_all = sums[-1]
    resid = sig32 - jnp.sum(correlations[:, None, None, None] * pmask, axis=0)
    eye = jnp.eye(nprior, dtype=jnp.float32)
    expanded = sig_sq_all + jnp.sum(correlations[:, None] * correlations[None, :] * (gram_all - 2.0 * eye))
    cells = sec_local * lax.axis_size("sec") * width * width

    def scaled(total):
        return (resid / jnp.sqrt(total / cells + 1e-06)).astype(jnp.bfloat16)

    fast = scaled(expanded)
    new_dir = lax.cond(
        expanded >= sig_sq_all * 0.0625,
        lambda r: fast,
        lambda r: scaled(small_sum(jnp.sum(r * r))),
        resid,
    )
    return (sigma, new_dir, correlations)


def solution(mesh):
    in_specs = (
        P("sec", None, None),
        P("ops", "sec", None, None),
        P("ops", "sec", None, None),
        P(None, "sec", "ops", None),
        P("sec"),
        P("sec"),
    )
    out_specs = (P("sec", "ops", None), P("sec", "ops", None), P())
    return jax.shard_map(shards, mesh=mesh, in_specs=in_specs, out_specs=out_specs, check_vma=False)
```

```python
import jax
import jax.numpy as jnp
from jax import lax
from jax.sharding import PartitionSpec as P


def reduce_rows(partial, shard_rows):
    n = lax.axis_size("ops")
    blocks = partial.reshape(n, shard_rows, partial.shape[2])
    got = lax.all_to_all(blocks, "ops", 0, 0, tiled=True)
    acc = got[0]
    for i in range(1, n):
        acc = acc + got[i]
    return acc[None]


def small_sum(v):
    for ax in ("sec", "ops"):
        n = lax.axis_size(ax)
        x = jnp.broadcast_to(v.reshape(1, -1), (n, v.size))
        v = jnp.sum(lax.all_to_all(x, ax, 0, 0, tiled=True), axis=0).reshape(v.shape)
    return v


def shards(wave, left_ops, right_ops, priors, row_sizes, col_sizes):
    width = wave.shape[1]
    sec_local = wave.shape[0]
    shard_rows = width // lax.axis_size("ops")
    first_row = lax.axis_index("ops") * shard_rows
    place = jnp.arange(width, dtype=jnp.int32)
    row_mask = (place[None, :] < row_sizes[:, None]).astype(jnp.float32)
    col_mask = (place[None, :] < col_sizes[:, None]).astype(jnp.float32)
    full_mask = row_mask[:, :, None] * col_mask[:, None, :]
    masked = wave * full_mask.astype(jnp.bfloat16)
    inner = lax.dot_general(
        masked[0], right_ops[0, 0], (((1,), (1,)), ((), ())), preferred_element_type=jnp.float32
    ).astype(jnp.bfloat16)
    partial_all = jnp.dot(left_ops[0, 0], inner, preferred_element_type=jnp.float32)[None]
    summed = reduce_rows(partial_all, shard_rows)
    mine_rows = lax.dynamic_slice_in_dim(row_mask, first_row, shard_rows, 1)
    mine_mask = mine_rows[:, :, None] * col_mask[:, None, :]
    own_rows = first_row + jnp.arange(shard_rows, dtype=jnp.int32)
    prior_ok = (own_rows[None, :, None] + 1 <= row_sizes[:, None, None]) & (
        place[None, None, :] + 1 <= col_sizes[:, None, None]
    )
    pmask = jnp.where(prior_ok[None], priors, jnp.zeros_like(priors)).astype(jnp.float32)
    gram = jnp.einsum("psab,qsab->pq", pmask, pmask, precision=lax.Precision.HIGHEST)
    sigma = (summed * mine_mask).astype(jnp.bfloat16)
    sig32 = sigma.astype(jnp.float32)
    local_over = jnp.sum(pmask * sig32[None], axis=(1, 2, 3))
    sig_sq = jnp.sum(sig32 * sig32)
    nprior = local_over.shape[0]
    packed = jnp.concatenate([local_over, gram.reshape(-1), sig_sq[None]])
    sums = small_sum(packed)
    correlations = sums[:nprior]
    gram_all = sums[nprior:-1].reshape(nprior, nprior)
    sig_sq_all = sums[-1]
    resid = sig32 - jnp.sum(correlations[:, None, None, None] * pmask, axis=0)
    eye = jnp.eye(nprior, dtype=jnp.float32)
    expanded = sig_sq_all + jnp.sum(correlations[:, None] * correlations[None, :] * (gram_all - 2.0 * eye))
    cells = sec_local * lax.axis_size("sec") * width * width

    def scaled(total):
        return (resid / jnp.sqrt(total / cells + 1e-06)).astype(jnp.bfloat16)

    fast = scaled(expanded)
    new_dir = lax.cond(
        expanded >= sig_sq_all * 0.0625,
        lambda r: fast,
        lambda r: scaled(small_sum(jnp.sum(r * r))),
        resid,
    )
    return (sigma, new_dir, correlations)


def solution(mesh):
    in_specs = (
        P("sec", None, None),
        P("ops", "sec", None, None),
        P("ops", "sec", None, None),
        P(None, "sec", "ops", None),
        P("sec"),
        P("sec"),
    )
    out_specs = (P("sec", "ops", None), P("sec", "ops", None), P())
    return jax.shard_map(shards, mesh=mesh, in_specs=in_specs, out_specs=out_specs, check_vma=False)
```

```python
import jax
import jax.numpy as jnp
from jax import lax
from jax.sharding import PartitionSpec as P


def reduce_rows(partial, shard_rows):
    n = lax.axis_size("ops")
    blocks = partial.reshape(n, shard_rows, partial.shape[2])
    got = lax.all_to_all(blocks, "ops", 0, 0, tiled=True)
    acc = got[0]
    for i in range(1, n):
        acc = acc + got[i]
    return acc[None]


def small_sum(v):
    for ax in ("sec", "ops"):
        n = lax.axis_size(ax)
        x = jnp.broadcast_to(v.reshape(1, -1), (n, v.size))
        v = jnp.sum(lax.all_to_all(x, ax, 0, 0, tiled=True), axis=0).reshape(v.shape)
    return v


def shards(wave, left_ops, right_ops, priors, row_sizes, col_sizes):
    width = wave.shape[1]
    sec_local = wave.shape[0]
    shard_rows = width // lax.axis_size("ops")
    first_row = lax.axis_index("ops") * shard_rows
    place = jnp.arange(width, dtype=jnp.int32)
    row_mask = (place[None, :] < row_sizes[:, None]).astype(jnp.float32)
    col_mask = (place[None, :] < col_sizes[:, None]).astype(jnp.float32)
    full_mask = row_mask[:, :, None] * col_mask[:, None, :]
    masked = wave * full_mask.astype(jnp.bfloat16)
    inner = lax.dot_general(
        masked[0], right_ops[0, 0], (((1,), (1,)), ((), ())), preferred_element_type=jnp.float32
    ).astype(jnp.bfloat16)
    partial_all = jnp.dot(left_ops[0, 0], inner, preferred_element_type=jnp.float32)[None]
    summed = reduce_rows(partial_all, shard_rows)
    mine_rows = lax.dynamic_slice_in_dim(row_mask, first_row, shard_rows, 1)
    mine_mask = mine_rows[:, :, None] * col_mask[:, None, :]
    own_rows = first_row + jnp.arange(shard_rows, dtype=jnp.int32)
    prior_ok = (own_rows[None, :, None] + 1 <= row_sizes[:, None, None]) & (
        place[None, None, :] + 1 <= col_sizes[:, None, None]
    )
    pmask = jnp.where(prior_ok[None], priors, jnp.zeros_like(priors)).astype(jnp.float32)
    gram = jnp.einsum("psab,qsab->pq", pmask, pmask, precision=lax.Precision.HIGHEST)
    sigma = (summed * mine_mask).astype(jnp.bfloat16)
    sig32 = sigma.astype(jnp.float32)
    local_over = jnp.sum(pmask * sig32[None], axis=(1, 2, 3))
    sig_sq = jnp.sum(sig32 * sig32)
    nprior = local_over.shape[0]
    packed = jnp.concatenate([local_over, gram.reshape(-1), sig_sq[None]])
    sums = small_sum(packed)
    correlations = sums[:nprior]
    gram_all = sums[nprior:-1].reshape(nprior, nprior)
    sig_sq_all = sums[-1]
    resid = sig32 - jnp.sum(correlations[:, None, None, None] * pmask, axis=0)
    eye = jnp.eye(nprior, dtype=jnp.float32)
    expanded = sig_sq_all + jnp.sum(
        correlations[:, None] * correlations[None, :] * (gram_all - 2.0 * eye), keepdims=True
    )
    cells = sec_local * lax.axis_size("sec") * width * width

    def scaled(total):
        return (resid / jnp.sqrt(total / cells + 1e-06)).astype(jnp.bfloat16)

    fast = scaled(expanded)
    new_dir = lax.cond(
        expanded[0, 0] >= sig_sq_all * 0.0625,
        lambda r: fast,
        lambda r: scaled(small_sum(jnp.sum(r * r, keepdims=True))),
        resid,
    )
    return (sigma, new_dir, correlations)


def solution(mesh):
    in_specs = (
        P("sec", None, None),
        P("ops", "sec", None, None),
        P("ops", "sec", None, None),
        P(None, "sec", "ops", None),
        P("sec"),
        P("sec"),
    )
    out_specs = (P("sec", "ops", None), P("sec", "ops", None), P())
    return jax.shard_map(shards, mesh=mesh, in_specs=in_specs, out_specs=out_specs, check_vma=False)
```

```python
import jax
import jax.numpy as jnp
from jax import lax
from jax.sharding import PartitionSpec as P


def reduce_rows(partial, shard_rows):
    n = lax.axis_size("ops")
    blocks = partial.reshape(n, shard_rows, partial.shape[2])
    got = lax.all_to_all(blocks, "ops", 0, 0, tiled=True)
    acc = got[0]
    for i in range(1, n):
        acc = acc + got[i]
    return acc[None]


def small_sum(v):
    for ax in ("sec", "ops"):
        n = lax.axis_size(ax)
        x = jnp.broadcast_to(v.reshape(1, -1), (n, v.size))
        v = jnp.sum(lax.all_to_all(x, ax, 0, 0, tiled=True), axis=0).reshape(v.shape)
    return v


def shards(wave, left_ops, right_ops, priors, row_sizes, col_sizes):
    width = wave.shape[1]
    sec_local = wave.shape[0]
    shard_rows = width // lax.axis_size("ops")
    first_row = lax.axis_index("ops") * shard_rows
    place = jnp.arange(width, dtype=jnp.int32)
    row_mask = (place[None, :] < row_sizes[:, None]).astype(jnp.float32)
    col_mask = (place[None, :] < col_sizes[:, None]).astype(jnp.float32)
    full_mask = row_mask[:, :, None] * col_mask[:, None, :]
    masked = wave * full_mask.astype(jnp.bfloat16)
    inner = lax.dot_general(
        masked[0], right_ops[0, 0], (((1,), (1,)), ((), ())), preferred_element_type=jnp.float32
    ).astype(jnp.bfloat16)
    partial_all = jnp.dot(left_ops[0, 0], inner, preferred_element_type=jnp.float32)[None]
    summed = reduce_rows(partial_all, shard_rows)
    mine_rows = lax.dynamic_slice_in_dim(row_mask, first_row, shard_rows, 1)
    mine_mask = mine_rows[:, :, None] * col_mask[:, None, :]
    own_rows = first_row + jnp.arange(shard_rows, dtype=jnp.int32)
    prior_ok = (own_rows[None, :, None] + 1 <= row_sizes[:, None, None]) & (
        place[None, None, :] + 1 <= col_sizes[:, None, None]
    )
    pmask = jnp.where(prior_ok[None], priors, jnp.zeros_like(priors)).astype(jnp.float32)
    gram = jnp.einsum("psab,qsab->pq", pmask, pmask, precision=lax.Precision.HIGHEST)
    sigma = (summed * mine_mask).astype(jnp.bfloat16)
    sig32 = sigma.astype(jnp.float32)
    stats = jnp.sum(jnp.concatenate([pmask, sig32[None]], axis=0) * sig32[None], axis=(1, 2, 3))
    nprior = pmask.shape[0]
    packed = jnp.concatenate([stats, gram.reshape(-1)])
    sums = small_sum(packed)
    correlations = sums[:nprior]
    sig_sq_all = sums[nprior]
    gram_all = sums[nprior + 1:].reshape(nprior, nprior)
    resid = sig32 - jnp.sum(correlations[:, None, None, None] * pmask, axis=0)
    eye = jnp.eye(nprior, dtype=jnp.float32)
    expanded = sig_sq_all + jnp.sum(
        correlations[:, None] * correlations[None, :] * (gram_all - 2.0 * eye), keepdims=True
    )
    cells = sec_local * lax.axis_size("sec") * width * width

    def scaled(total):
        return (resid / jnp.sqrt(total / cells + 1e-06)).astype(jnp.bfloat16)

    fast = scaled(expanded)
    new_dir = lax.cond(
        expanded[0, 0] >= sig_sq_all * 0.0625,
        lambda r: fast,
        lambda r: scaled(small_sum(jnp.sum(r * r, keepdims=True))),
        resid,
    )
    return (sigma, new_dir, correlations)


def solution(mesh):
    in_specs = (
        P("sec", None, None),
        P("ops", "sec", None, None),
        P("ops", "sec", None, None),
        P(None, "sec", "ops", None),
        P("sec"),
        P("sec"),
    )
    out_specs = (P("sec", "ops", None), P("sec", "ops", None), P())
    return jax.shard_map(shards, mesh=mesh, in_specs=in_specs, out_specs=out_specs, check_vma=False)
```
